256 devices in a mesh: row: 8 (over y, core), col: 32 (over x, z).
Axes of the slice: x: 4, y: 4, z: 8, core: 2. Of those that a mesh axis runs over, the one named last changes fastest.
Arguments:
- density: float32 [512, 1024, 128], P('row', 'col'), may hold values from 0 to 40, as said below
Outputs:
- coarse: float32 [512, 1024, 128], P('row', 'col')
- moments: float32 [3, 4, 2, 4], replicated
The draws below stay inside these ranges and needn't reach their ends.
Inputs may be any that keep to these rules, and one draw needn't show every extreme that they name: Positive density.
All inputs are finite; a program needn't handle non-finite values.
Results may differ from the reference program's by a relative error of at most 0.0003.
Values sent between devices are 32-bit elements; how exact they have to be, the bound alone decides.
No kernel may reach another device: no remote copies, remote signals or barrier semaphores. Data moves between devices by JAX's collectives and lax.ppermute only.
A program may use at most 64 MiB of HBM per device.

```python
import jax
import jax.numpy as jnp

NZ = 128
SUB = 256
NX = 512
NY = 1024
NSX = 2
NSY = 4


def draw_density(key, part):
    shape = (NX, NY, NZ)
    first_key = jax.random.fold_in(key, 11)
    xs_coord = jnp.arange(NX, dtype=jnp.float32)[:, None, None]
    ys_coord = jnp.arange(NY, dtype=jnp.float32)[None, :, None]
    amp_x = 0.6 * (1.0 + 2.0 * (jnp.mod(xs_coord, SUB) + 0.5) / SUB)
    amp_y = 1.0 + 0.5 * (jnp.mod(ys_coord, SUB) + 0.5) / SUB
    noise = jax.random.truncated_normal(first_key, -4.0, 4.0, shape, jnp.float32)
    return amp_x * amp_y * jnp.exp(0.5 * noise)


def setup_inputs(seed: int = 0) -> dict:
    keys = jax.random.split(jax.random.key(seed), 2)
    density = draw_density(jax.random.fold_in(keys[1], 71), 0)
    return {"density": density}


SPLINE_TAPS = (0.0625, 0.25, 0.375, 0.25, 0.0625)
SPACINGS = (4, 8, 16)
EPSILON = 1e-6


def rolled_pass(values_in, spacing, axis_number):
    summed = SPLINE_TAPS[0] * jnp.roll(values_in, 2 * spacing, axis=axis_number)
    for tap_index in (1, 2, 3, 4):
        summed = summed + SPLINE_TAPS[tap_index] * jnp.roll(values_in, -(tap_index - 2) * spacing, axis=axis_number)
    return summed


def depth_pass(values_in, spacing):
    summed = SPLINE_TAPS[2] * values_in
    for tap_index in (0, 1, 3, 4):
        summed = summed + SPLINE_TAPS[tap_index] * jnp.roll(values_in, -(tap_index - 2) * spacing, axis=2)
    return summed


def finish_table(table, planes):
    means = table / jnp.float32(SUB * SUB * planes)
    second = means[:, 1]
    third = means[:, 2] / (second + EPSILON) ** 1.5
    fourth = means[:, 3] / (second + EPSILON) ** 2
    return jnp.stack([means[:, 0], second, third, fourth], axis=1)


def reference(density):
    current = density
    tables = []
    for spacing in SPACINGS:
        along_x = rolled_pass(current, spacing, 0)
        along_y = rolled_pass(along_x, spacing, 1)
        smoother = depth_pass(along_y, spacing)
        detail = (current - smoother).reshape(NSX, SUB, NSY, SUB, NZ)
        square = detail * detail
        tables.append(jnp.stack([
            jnp.sum(jnp.abs(detail), axis=(1, 3, 4)),
            jnp.sum(square, axis=(1, 3, 4)),
            jnp.sum(square * detail, axis=(1, 3, 4)),
            jnp.sum(square * square, axis=(1, 3, 4))]))
        current = smoother
    table = jnp.stack(tables)
    return current, finish_table(table, NZ)
```

```python
import jax
import jax.numpy as jnp
from jax import lax
from jax.sharding import PartitionSpec as P

SUB = 256


SPLINE_TAPS = (0.0625, 0.25, 0.375, 0.25, 0.0625)
SPACINGS = (4, 8, 16)
EPSILON = 1e-06


def ring_pairs(count):
    forward = [(i, (i + 1) % count) for i in range(count)]
    backward = [(target, source) for source, target in forward]
    return forward, backward


def padded_1(block, axis, dim, width):
    count = lax.axis_size(axis)
    assert width <= block.shape[dim]
    forward, backward = ring_pairs(count)
    low = lax.ppermute(
        lax.slice_in_dim(block, block.shape[dim] - width, None, axis=dim), axis, forward
    )
    high = lax.ppermute(lax.slice_in_dim(block, 0, width, axis=dim), axis, backward)
    return jnp.concatenate([low, block, high], axis=dim)


def holed_pass(padded, spacing, axis_number, length_out):
    summed = SPLINE_TAPS[0] * lax.slice_in_dim(padded, 0, length_out, axis=axis_number)
    for tap_index in (1, 2, 3, 4):
        portion = lax.slice_in_dim(
            padded, tap_index * spacing, tap_index * spacing + length_out, axis=axis_number
        )
        summed = summed + SPLINE_TAPS[tap_index] * portion
    return summed


def depth_pass(values_in, spacing):
    summed = SPLINE_TAPS[2] * values_in
    for tap_index in (0, 1, 3, 4):
        summed = summed + SPLINE_TAPS[tap_index] * jnp.roll(
            values_in, -(tap_index - 2) * spacing, axis=2
        )
    return summed


def moment_sums(detail):
    square = detail * detail
    return jnp.stack(
        [
            jnp.sum(jnp.abs(detail)),
            jnp.sum(square),
            jnp.sum(square * detail),
            jnp.sum(square * square),
        ]
    )


def finish_table(table, planes):
    means = table / jnp.float32(SUB * SUB * planes)
    second = means[:, 1]
    third = means[:, 2] / (second + EPSILON) ** 1.5
    fourth = means[:, 3] / (second + EPSILON) ** 2
    return jnp.stack([means[:, 0], second, third, fourth], axis=1)


def butterfly_sum(table, axes):
    for axis in axes:
        count = lax.axis_size(axis)
        assert count & (count - 1) == 0
        step = 1
        while step < count:
            pairs = [(i, i ^ step) for i in range(count)]
            table = table + lax.ppermute(table, axis, pairs)
            step *= 2
    return table


def per_device(density):
    size_x, size_y, planes = density.shape
    assert SUB % size_x == 0 and SUB % size_y == 0
    sums = []
    current = density
    for spacing in SPACINGS:
        padded_x = padded_1(current, "row", 0, 2 * spacing)
        along_x = holed_pass(padded_x, spacing, 0, size_x)
        padded_y = padded_1(along_x, "col", 1, 2 * spacing)
        along_y = holed_pass(padded_y, spacing, 1, size_y)
        smoother = depth_pass(along_y, spacing)
        sums.append(moment_sums(current - smoother))
        current = smoother
    partial = jnp.stack(sums)
    count_x = lax.axis_size("row") * size_x // SUB
    count_y = lax.axis_size("col") * size_y // SUB
    block_x = lax.axis_index("row") * size_x // SUB
    block_y = lax.axis_index("col") * size_y // SUB
    onehot_x = (jnp.arange(count_x, dtype=jnp.int32) == block_x).astype(jnp.float32)
    onehot_y = (jnp.arange(count_y, dtype=jnp.int32) == block_y).astype(jnp.float32)
    partial_table = (
        partial[:, :, None, None] * onehot_x[None, None, :, None] * onehot_y[None, None, None, :]
    )
    table = butterfly_sum(partial_table, ("row", "col"))
    return (current, finish_table(table, planes))


def solution(mesh):
    placed = (P("row", "col", None),)
    return jax.shard_map(
        per_device,
        mesh=mesh,
        in_specs=placed,
        out_specs=(P("row", "col", None), P()),
        check_vma=False,
    )
```

```python
import jax
import jax.numpy as jnp
from jax import lax
from jax.sharding import PartitionSpec as P

SUB = 256


SPLINE_TAPS = (0.0625, 0.25, 0.375, 0.25, 0.0625)
SPACINGS = (4, 8, 16)
EPSILON = 1e-06


def ring_pairs(count):
    forward = [(i, (i + 1) % count) for i in range(count)]
    backward = [(target, source) for source, target in forward]
    return forward, backward


def padded_1(block, axis, dim, width):
    count = lax.axis_size(axis)
    assert width <= block.shape[dim]
    forward, backward = ring_pairs(count)
    low = lax.ppermute(
        lax.slice_in_dim(block, block.shape[dim] - width, None, axis=dim), axis, forward
    )
    high = lax.ppermute(lax.slice_in_dim(block, 0, width, axis=dim), axis, backward)
    return jnp.concatenate([low, block, high], axis=dim)


def holed_pass(padded, spacing, axis_number, length_out):
    summed = SPLINE_TAPS[0] * lax.slice_in_dim(padded, 0, length_out, axis=axis_number)
    for tap_index in (1, 2, 3, 4):
        portion = lax.slice_in_dim(
            padded, tap_index * spacing, tap_index * spacing + length_out, axis=axis_number
        )
        summed = summed + SPLINE_TAPS[tap_index] * portion
    return summed


def depth_pass(values_in, spacing):
    summed = SPLINE_TAPS[2] * values_in
    for tap_index in (0, 1, 3, 4):
        summed = summed + SPLINE_TAPS[tap_index] * jnp.roll(
            values_in, -(tap_index - 2) * spacing, axis=2
        )
    return summed


def moment_sums(detail):
    square = detail * detail
    powers = jnp.stack([jnp.abs(detail), square, square * detail, square * square])
    return jnp.sum(powers.reshape(4, -1), axis=1)


def finish_table(table, planes):
    means = table / jnp.float32(SUB * SUB * planes)
    second = means[:, 1]
    third = means[:, 2] / (second + EPSILON) ** 1.5
    fourth = means[:, 3] / (second + EPSILON) ** 2
    return jnp.stack([means[:, 0], second, third, fourth], axis=1)


def gather_partials(partial, axes):
    count = 1
    for axis in axes:
        count *= lax.axis_size(axis)
    flat = partial.reshape(1, -1)
    sent = jnp.broadcast_to(flat, (count, flat.shape[1]))
    return lax.all_to_all(sent, axes, 0, 0, tiled=True)


def per_device(density):
    size_x, size_y, planes = density.shape
    assert SUB % size_x == 0 and SUB % size_y == 0
    sums = []
    current = density
    for spacing in SPACINGS:
        padded_x = padded_1(current, "row", 0, 2 * spacing)
        along_x = holed_pass(padded_x, spacing, 0, size_x)
        padded_y = padded_1(along_x, "col", 1, 2 * spacing)
        along_y = holed_pass(padded_y, spacing, 1, size_y)
        smoother = depth_pass(along_y, spacing)
        sums.append(moment_sums(current - smoother))
        current = smoother
    partial = jnp.stack(sums)
    count_x = lax.axis_size("row") * size_x // SUB
    count_y = lax.axis_size("col") * size_y // SUB
    gathered = gather_partials(partial, ("row", "col"))
    per_x = SUB // size_x
    per_y = SUB // size_y
    grouped = gathered.reshape(count_x, per_x, count_y, per_y, len(SPACINGS), 4)
    table = jnp.transpose(jnp.sum(grouped, axis=(1, 3)), (2, 3, 0, 1))
    return (current, finish_table(table, planes))


def solution(mesh):
    placed = (P("row", "col", None),)
    return jax.shard_map(
        per_device,
        mesh=mesh,
        in_specs=placed,
        out_specs=(P("row", "col", None), P()),
        check_vma=False,
    )
```

```python
import jax
import jax.numpy as jnp
import numpy as np
from jax import lax
from jax.sharding import PartitionSpec as P

SUB = 256


SPLINE_TAPS = (0.0625, 0.25, 0.375, 0.25, 0.0625)
SPACINGS = (4, 8, 16)
EPSILON = 1e-06


def ring_pairs(count):
    forward = [(i, (i + 1) % count) for i in range(count)]
    backward = [(target, source) for source, target in forward]
    return forward, backward


def padded_1(block, axis, dim, width):
    count = lax.axis_size(axis)
    assert width <= block.shape[dim]
    forward, backward = ring_pairs(count)
    low = lax.ppermute(
        lax.slice_in_dim(block, block.shape[dim] - width, None, axis=dim), axis, forward
    )
    high = lax.ppermute(lax.slice_in_dim(block, 0, width, axis=dim), axis, backward)
    return jnp.concatenate([low, block, high], axis=dim)


def holed_pass(padded, spacing, axis_number, length_out):
    summed = SPLINE_TAPS[0] * lax.slice_in_dim(padded, 0, length_out, axis=axis_number)
    for tap_index in (1, 2, 3, 4):
        portion = lax.slice_in_dim(
            padded, tap_index * spacing, tap_index * spacing + length_out, axis=axis_number
        )
        summed = summed + SPLINE_TAPS[tap_index] * portion
    return summed


def depth_matrix(planes, spacing):
    matrix = np.zeros((planes, planes), np.float32)
    for tap_index in range(5):
        for i in range(planes):
            matrix[(i + (tap_index - 2) * spacing) % planes, i] += SPLINE_TAPS[tap_index]
    return matrix


def depth_pass(values_in, spacing):
    rows = values_in.shape[:-1]
    planes = values_in.shape[-1]
    flat = values_in.reshape(-1, planes)
    summed = jnp.dot(
        flat,
        jnp.asarray(depth_matrix(planes, spacing)),
        precision=lax.Precision.HIGHEST,
        preferred_element_type=jnp.float32,
    )
    return summed.reshape(*rows, planes)


def moment_sums(detail):
    square = detail * detail
    return jnp.stack(
        [
            jnp.sum(jnp.abs(detail), axis=(0, 1)),
            jnp.sum(square, axis=(0, 1)),
            jnp.sum(square * detail, axis=(0, 1)),
            jnp.sum(square * square, axis=(0, 1)),
        ]
    )


def finish_table(table, planes):
    means = table / jnp.float32(SUB * SUB * planes)
    second = means[:, 1]
    third = means[:, 2] / (second + EPSILON) ** 1.5
    fourth = means[:, 3] / (second + EPSILON) ** 2
    return jnp.stack([means[:, 0], second, third, fourth], axis=1)


def gather_partials(partial, axes):
    count = 1
    for axis in axes:
        count *= lax.axis_size(axis)
    flat = partial.reshape(1, -1)
    sent = jnp.broadcast_to(flat, (count, flat.shape[1]))
    return lax.all_to_all(sent, axes, 0, 0, tiled=True)


def per_device(density):
    size_x, size_y, planes = density.shape
    assert SUB % size_x == 0 and SUB % size_y == 0
    sums = []
    current = density
    for spacing in SPACINGS:
        padded_x = padded_1(current, "row", 0, 2 * spacing)
        along_x = holed_pass(padded_x, spacing, 0, size_x)
        padded_y = padded_1(along_x, "col", 1, 2 * spacing)
        along_y = holed_pass(padded_y, spacing, 1, size_y)
        smoother = depth_pass(along_y, spacing)
        sums.append(moment_sums(current - smoother))
        current = smoother
    partial = jnp.sum(jnp.stack(sums), axis=-1)
    count_x = lax.axis_size("row") * size_x // SUB
    count_y = lax.axis_size("col") * size_y // SUB
    gathered = gather_partials(partial, ("row", "col"))
    per_x = SUB // size_x
    per_y = SUB // size_y
    grouped = gathered.reshape(count_x, per_x, count_y, per_y, len(SPACINGS), 4)
    table = jnp.transpose(jnp.sum(grouped, axis=(1, 3)), (2, 3, 0, 1))
    return (current, finish_table(table, planes))


def solution(mesh):
    placed = (P("row", "col", None),)
    return jax.shard_map(
        per_device,
        mesh=mesh,
        in_specs=placed,
        out_specs=(P("row", "col", None), P()),
        check_vma=False,
    )
```

```python
import jax
import jax.numpy as jnp
import numpy as np
from jax import lax
from jax.sharding import PartitionSpec as P

SUB = 256


SPLINE_TAPS = (0.0625, 0.25, 0.375, 0.25, 0.0625)
SPACINGS = (4, 8, 16)
EPSILON = 1e-06
ONE_ROUND = (4,)


def ring_pairs(count):
    forward = [(i, (i + 1) % count) for i in range(count)]
    backward = [(target, source) for source, target in forward]
    return forward, backward


def padded_1(block, axis, dim, width):
    count = lax.axis_size(axis)
    assert width <= block.shape[dim]
    forward, backward = ring_pairs(count)
    low = lax.ppermute(
        lax.slice_in_dim(block, block.shape[dim] - width, None, axis=dim), axis, forward
    )
    high = lax.ppermute(lax.slice_in_dim(block, 0, width, axis=dim), axis, backward)
    return jnp.concatenate([low, block, high], axis=dim)


def padded_both(block, width):
    rows = lax.axis_size("row")
    cols = lax.axis_size("col")
    size_x, size_y = block.shape[0], block.shape[1]
    assert width <= size_x and width <= size_y

    def shifted(piece, dr, dc):
        if dc == 0:
            return lax.ppermute(piece, "row", [(i, (i + dr) % rows) for i in range(rows)])
        if dr == 0:
            return lax.ppermute(piece, "col", [(i, (i + dc) % cols) for i in range(cols)])
        pairs = [
            (r * cols + c, ((r + dr) % rows) * cols + (c + dc) % cols)
            for r in range(rows)
            for c in range(cols)
        ]
        return lax.ppermute(piece, ("row", "col"), pairs)

    top = slice(size_x - width, size_x)
    bottom = slice(0, width)
    right_edge = slice(size_y - width, size_y)
    left_edge = slice(0, width)
    full = slice(None)
    up = shifted(block[top, full], 1, 0)
    down = shifted(block[bottom, full], -1, 0)
    left = shifted(block[full, right_edge], 0, 1)
    right = shifted(block[full, left_edge], 0, -1)
    up_left = shifted(block[top, right_edge], 1, 1)
    up_right = shifted(block[top, left_edge], 1, -1)
    down_left = shifted(block[bottom, right_edge], -1, 1)
    down_right = shifted(block[bottom, left_edge], -1, -1)
    return jnp.concatenate(
        [
            jnp.concatenate([up_left, up, up_right], axis=1),
            jnp.concatenate([left, block, right], axis=1),
            jnp.concatenate([down_left, down, down_right], axis=1),
        ],
        axis=0,
    )


def holed_pass(padded, spacing, axis_number, length_out):
    summed = SPLINE_TAPS[0] * lax.slice_in_dim(padded, 0, length_out, axis=axis_number)
    for tap_index in (1, 2, 3, 4):
        portion = lax.slice_in_dim(
            padded, tap_index * spacing, tap_index * spacing + length_out, axis=axis_number
        )
        summed = summed + SPLINE_TAPS[tap_index] * portion
    return summed


def depth_matrix(planes, spacing):
    matrix = np.zeros((planes, planes), np.float32)
    for tap_index in range(5):
        for i in range(planes):
            matrix[(i + (tap_index - 2) * spacing) % planes, i] += SPLINE_TAPS[tap_index]
    return matrix


def depth_pass(values_in, spacing):
    rows = values_in.shape[:-1]
    planes = values_in.shape[-1]
    flat = values_in.reshape(-1, planes)
    summed = jnp.dot(
        flat,
        jnp.asarray(depth_matrix(planes, spacing)),
        precision=lax.Precision.HIGHEST,
        preferred_element_type=jnp.float32,
    )
    return summed.reshape(*rows, planes)


def moment_sums(detail):
    square = detail * detail
    return jnp.stack(
        [
            jnp.sum(jnp.abs(detail), axis=(0, 1)),
            jnp.sum(square, axis=(0, 1)),
            jnp.sum(square * detail, axis=(0, 1)),
            jnp.sum(square * square, axis=(0, 1)),
        ]
    )


def finish_table(table, planes):
    means = table / jnp.float32(SUB * SUB * planes)
    second = means[:, 1]
    third = means[:, 2] / (second + EPSILON) ** 1.5
    fourth = means[:, 3] / (second + EPSILON) ** 2
    return jnp.stack([means[:, 0], second, third, fourth], axis=1)


def gather_partials(partial, axes):
    count = 1
    for axis in axes:
        count *= lax.axis_size(axis)
    flat = partial.reshape(1, -1)
    sent = jnp.broadcast_to(flat, (count, flat.shape[1]))
    return lax.all_to_all(sent, axes, 0, 0, tiled=True)


def per_device(density):
    size_x, size_y, planes = density.shape
    assert SUB % size_x == 0 and SUB % size_y == 0
    sums = []
    current = density
    for spacing in SPACINGS:
        if spacing in ONE_ROUND:
            padded = padded_both(current, 2 * spacing)
            along_y = holed_pass(holed_pass(padded, spacing, 0, size_x), spacing, 1, size_y)
        else:
            padded_x = padded_1(current, "row", 0, 2 * spacing)
            along_x = holed_pass(padded_x, spacing, 0, size_x)
            padded_y = padded_1(along_x, "col", 1, 2 * spacing)
            along_y = holed_pass(padded_y, spacing, 1, size_y)
        smoother = depth_pass(along_y, spacing)
        sums.append(moment_sums(current - smoother))
        current = smoother
    partial = jnp.sum(jnp.stack(sums), axis=-1)
    count_x = lax.axis_size("row") * size_x // SUB
    count_y = lax.axis_size("col") * size_y // SUB
    gathered = gather_partials(partial, ("row", "col"))
    per_x = SUB // size_x
    per_y = SUB // size_y
    grouped = gathered.reshape(count_x, per_x, count_y, per_y, len(SPACINGS), 4)
    table = jnp.transpose(jnp.sum(grouped, axis=(1, 3)), (2, 3, 0, 1))
    return (current, finish_table(table, planes))


def solution(mesh):
    placed = (P("row", "col", None),)
    return jax.shard_map(
        per_device,
        mesh=mesh,
        in_specs=placed,
        out_specs=(P("row", "col", None), P()),
        check_vma=False,
    )
```

```python
import jax
import jax.numpy as jnp
import numpy as np
from jax import lax
from jax.sharding import PartitionSpec as P


SUB = 256


SPLINE_TAPS = (0.0625, 0.25, 0.375, 0.25, 0.0625)
SPACINGS = (4, 8, 16)
EPSILON = 1e-06


def ring_pairs(count):
    forward = [(i, (i + 1) % count) for i in range(count)]
    backward = [(target, source) for source, target in forward]
    return forward, backward


def edges_1(block, axis, dim, width):
    count = lax.axis_size(axis)
    assert width <= block.shape[dim]
    forward, backward = ring_pairs(count)
    low = lax.ppermute(
        lax.slice_in_dim(block, block.shape[dim] - width, None, axis=dim), axis, forward
    )
    high = lax.ppermute(lax.slice_in_dim(block, 0, width, axis=dim), axis, backward)
    return low, high


def padded_1(block, axis, dim, width):
    count = lax.axis_size(axis)
    assert width <= block.shape[dim]
    forward, backward = ring_pairs(count)
    low = lax.ppermute(
        lax.slice_in_dim(block, block.shape[dim] - width, None, axis=dim), axis, forward
    )
    high = lax.ppermute(lax.slice_in_dim(block, 0, width, axis=dim), axis, backward)
    return jnp.concatenate([low, block, high], axis=dim)


def holed_pass(padded, spacing, axis_number, length_out):
    summed = SPLINE_TAPS[0] * lax.slice_in_dim(padded, 0, length_out, axis=axis_number)
    for tap_index in (1, 2, 3, 4):
        portion = lax.slice_in_dim(
            padded, tap_index * spacing, tap_index * spacing + length_out, axis=axis_number
        )
        summed = summed + SPLINE_TAPS[tap_index] * portion
    return summed


def depth_matrix(planes, spacing):
    matrix = np.zeros((planes, planes), np.float32)
    for tap_index in range(5):
        for i in range(planes):
            matrix[(i + (tap_index - 2) * spacing) % planes, i] += SPLINE_TAPS[tap_index]
    return matrix


def depth_pass(values_in, spacing):
    rows = values_in.shape[:-1]
    planes = values_in.shape[-1]
    flat = values_in.reshape(-1, planes)
    summed = jnp.dot(
        flat,
        jnp.asarray(depth_matrix(planes, spacing)),
        precision=lax.Precision.HIGHEST,
        preferred_element_type=jnp.float32,
    )
    return summed.reshape(*rows, planes)


def moment_sums(detail):
    square = detail * detail
    return jnp.stack(
        [
            jnp.sum(jnp.abs(detail), axis=(0, 1)),
            jnp.sum(square, axis=(0, 1)),
            jnp.sum(square * detail, axis=(0, 1)),
            jnp.sum(square * square, axis=(0, 1)),
        ]
    )


def finish_table(table, planes):
    means = table / jnp.float32(SUB * SUB * planes)
    second = means[:, 1]
    third = means[:, 2] / (second + EPSILON) ** 1.5
    fourth = means[:, 3] / (second + EPSILON) ** 2
    return jnp.stack([means[:, 0], second, third, fourth], axis=1)


def gather_partials(partial, axes):
    count = 1
    for axis in axes:
        count *= lax.axis_size(axis)
    flat = partial.reshape(1, -1)
    sent = jnp.broadcast_to(flat, (count, flat.shape[1]))
    return lax.all_to_all(sent, axes, 0, 0, tiled=True)


def per_device(density):
    size_x, size_y, planes = density.shape
    assert SUB % size_x == 0 and SUB % size_y == 0
    sums = []
    current = density
    for spacing in SPACINGS:
      width = 2 * spacing
      padded_x = padded_1(current, "row", 0, width)
      along_x = holed_pass(padded_x, spacing, 0, size_x)
      if size_x > 2 * width:
          inner = holed_pass(current, spacing, 0, size_x - 2 * width)
          inner_low, inner_high = edges_1(inner, "col", 1, width)
          rims = jnp.concatenate([along_x[:width], along_x[size_x - width :]], axis=0)
          rim_low, rim_high = edges_1(rims, "col", 1, width)
          low = jnp.concatenate([rim_low[:width], inner_low, rim_low[width:]], axis=0)
          high = jnp.concatenate([rim_high[:width], inner_high, rim_high[width:]], axis=0)
          padded_y = jnp.concatenate([low, along_x, high], axis=1)
      else:
          padded_y = padded_1(along_x, "col", 1, width)
      along_y = holed_pass(padded_y, spacing, 1, size_y)
      smoother = depth_pass(along_y, spacing)
      sums.append(moment_sums(current - smoother))
      current = smoother
    partial = jnp.sum(jnp.stack(sums), axis=-1)
    count_x = lax.axis_size("row") * size_x // SUB
    count_y = lax.axis_size("col") * size_y // SUB
    gathered = gather_partials(partial, ("row", "col"))
    per_x = SUB // size_x
    per_y = SUB // size_y
    grouped = gathered.reshape(count_x, per_x, count_y, per_y, len(SPACINGS), 4)
    table = jnp.transpose(jnp.sum(grouped, axis=(1, 3)), (2, 3, 0, 1))
    return (current, finish_table(table, planes))


def solution(mesh):
    placed = (P("row", "col", None),)
    return jax.shard_map(
        per_device,
        mesh=mesh,
        in_specs=placed,
        out_specs=(P("row", "col", None), P()),
        check_vma=False,
    )
```

```python
import jax
import jax.numpy as jnp
import numpy as np
from jax import lax
from jax.sharding import PartitionSpec as P

SUB = 256


SPLINE_TAPS = (0.0625, 0.25, 0.375, 0.25, 0.0625)
SPACINGS = (4, 8, 16)
EPSILON = 1e-06


def ring_pairs(count):
    forward = [(i, (i + 1) % count) for i in range(count)]
    backward = [(target, source) for source, target in forward]
    return forward, backward


def padded_1(block, axis, dim, width):
    count = lax.axis_size(axis)
    assert width <= block.shape[dim]
    forward, backward = ring_pairs(count)
    low = lax.ppermute(
        lax.slice_in_dim(block, block.shape[dim] - width, None, axis=dim), axis, forward
    )
    high = lax.ppermute(lax.slice_in_dim(block, 0, width, axis=dim), axis, backward)
    return jnp.concatenate([low, block, high], axis=dim)


def holed_pass(padded, spacing, axis_number, length_out):
    summed = SPLINE_TAPS[0] * lax.slice_in_dim(padded, 0, length_out, axis=axis_number)
    for tap_index in (1, 2, 3, 4):
        portion = lax.slice_in_dim(
            padded, tap_index * spacing, tap_index * spacing + length_out, axis=axis_number
        )
        summed = summed + SPLINE_TAPS[tap_index] * portion
    return summed


def depth_matrix(planes, spacing):
    matrix = np.zeros((planes, planes), np.float32)
    for tap_index in range(5):
        for i in range(planes):
            matrix[(i + (tap_index - 2) * spacing) % planes, i] += SPLINE_TAPS[tap_index]
    return matrix


def depth_pass(values_in, spacing):
    rows = values_in.shape[:-1]
    planes = values_in.shape[-1]
    flat = values_in.reshape(-1, planes)
    summed = jnp.dot(
        flat,
        jnp.asarray(depth_matrix(planes, spacing)),
        precision=lax.Precision.HIGHEST,
        preferred_element_type=jnp.float32,
    )
    return summed.reshape(*rows, planes)


def moment_sums(detail):
    square = detail * detail
    return jnp.stack(
        [
            jnp.sum(jnp.abs(detail), axis=(0, 1)),
            jnp.sum(square, axis=(0, 1)),
            jnp.sum(square * detail, axis=(0, 1)),
            jnp.sum(square * square, axis=(0, 1)),
        ]
    )


def finish_table(table, planes):
    means = table / jnp.float32(SUB * SUB * planes)
    second = means[:, 1:2]
    column = lax.broadcasted_iota(jnp.int32, means.shape, 1)
    ones = jnp.ones_like(means)
    scale = jnp.where(
        column == 2, (second + EPSILON) ** 1.5, jnp.where(column == 3, (second + EPSILON) ** 2, ones)
    )
    return means / scale


def gather_partials(partial, axes):
    count = 1
    for axis in axes:
        count *= lax.axis_size(axis)
    flat = partial.reshape(1, -1)
    sent = jnp.broadcast_to(flat, (count, flat.shape[1]))
    return lax.all_to_all(sent, axes, 0, 0, tiled=True)


def per_device(density):
    size_x, size_y, planes = density.shape
    assert SUB % size_x == 0 and SUB % size_y == 0
    sums = []
    current = density
    for spacing in SPACINGS:
        padded_x = padded_1(current, "row", 0, 2 * spacing)
        along_x = holed_pass(padded_x, spacing, 0, size_x)
        padded_y = padded_1(along_x, "col", 1, 2 * spacing)
        along_y = holed_pass(padded_y, spacing, 1, size_y)
        smoother = depth_pass(along_y, spacing)
        sums.append(moment_sums(current - smoother))
        current = smoother
    partial = jnp.sum(jnp.stack(sums), axis=-1)
    count_x = lax.axis_size("row") * size_x // SUB
    count_y = lax.axis_size("col") * size_y // SUB
    gathered = gather_partials(partial, ("row", "col"))
    rows, cols = lax.axis_size("row"), lax.axis_size("col")
    owner = np.zeros((count_x * count_y, rows * cols), np.float32)
    for r in range(rows):
        for c in range(cols):
            owner[(r * size_x // SUB) * count_y + c * size_y // SUB, r * cols + c] = 1.0
    summed = jnp.dot(
        jnp.asarray(owner), gathered, precision=lax.Precision.HIGHEST,
        preferred_element_type=jnp.float32,
    )
    table = jnp.transpose(summed.reshape(count_x, count_y, len(SPACINGS), 4), (2, 3, 0, 1))
    return (current, finish_table(table, planes))


def solution(mesh):
    placed = (P("row", "col", None),)
    return jax.shard_map(
        per_device,
        mesh=mesh,
        in_specs=placed,
        out_specs=(P("row", "col", None), P()),
        check_vma=False,
    )
```

```python
import jax
import jax.numpy as jnp
import numpy as np
from jax import lax
from jax.sharding import PartitionSpec as P

SUB = 256


SPLINE_TAPS = (0.0625, 0.25, 0.375, 0.25, 0.0625)
SPACINGS = (4, 8, 16)
EPSILON = 1e-06
REACH_AHEAD = (1,)


def ring_pairs(count):
    forward = [(i, (i + 1) % count) for i in range(count)]
    backward = [(target, source) for source, target in forward]
    return forward, backward


def padded_1(block, axis, dim, width):
    count = lax.axis_size(axis)
    assert width <= block.shape[dim]
    forward, backward = ring_pairs(count)
    low = lax.ppermute(
        lax.slice_in_dim(block, block.shape[dim] - width, None, axis=dim), axis, forward
    )
    high = lax.ppermute(lax.slice_in_dim(block, 0, width, axis=dim), axis, backward)
    return jnp.concatenate([low, block, high], axis=dim)


def holed_pass(padded, spacing, axis_number, length_out):
    summed = SPLINE_TAPS[0] * lax.slice_in_dim(padded, 0, length_out, axis=axis_number)
    for tap_index in (1, 2, 3, 4):
        portion = lax.slice_in_dim(
            padded, tap_index * spacing, tap_index * spacing + length_out, axis=axis_number
        )
        summed = summed + SPLINE_TAPS[tap_index] * portion
    return summed


def depth_matrix(planes, spacing):
    matrix = np.zeros((planes, planes), np.float32)
    for tap_index in range(5):
        for i in range(planes):
            matrix[(i + (tap_index - 2) * spacing) % planes, i] += SPLINE_TAPS[tap_index]
    return matrix


def depth_pass(values_in, spacing):
    rows = values_in.shape[:-1]
    planes = values_in.shape[-1]
    flat = values_in.reshape(-1, planes)
    summed = jnp.dot(
        flat,
        jnp.asarray(depth_matrix(planes, spacing)),
        precision=lax.Precision.HIGHEST,
        preferred_element_type=jnp.float32,
    )
    return summed.reshape(*rows, planes)


def moment_sums(detail):
    square = detail * detail
    return jnp.stack(
        [
            jnp.sum(jnp.abs(detail), axis=(0, 1)),
            jnp.sum(square, axis=(0, 1)),
            jnp.sum(square * detail, axis=(0, 1)),
            jnp.sum(square * square, axis=(0, 1)),
        ]
    )


def finish_table(table, planes):
    means = table / jnp.float32(SUB * SUB * planes)
    second = means[:, 1:2]
    column = lax.broadcasted_iota(jnp.int32, means.shape, 1)
    ones = jnp.ones_like(means)
    scale = jnp.where(
        column == 2, (second + EPSILON) ** 1.5, jnp.where(column == 3, (second + EPSILON) ** 2, ones)
    )
    return means / scale


def gather_partials(partial, axes):
    count = 1
    for axis in axes:
        count *= lax.axis_size(axis)
    flat = partial.reshape(1, -1)
    sent = jnp.broadcast_to(flat, (count, flat.shape[1]))
    return lax.all_to_all(sent, axes, 0, 0, tiled=True)


def per_device(density):
    size_x, size_y, planes = density.shape
    assert SUB % size_x == 0 and SUB % size_y == 0
    sums = []
    current = density
    padded_x = None
    for scale, spacing in enumerate(SPACINGS):
        width = 2 * spacing
        extra = 2 * SPACINGS[scale + 1] if scale + 1 in REACH_AHEAD else 0
        if padded_x is None:
            padded_x = padded_1(current, "row", 0, width + extra)
        along_x = holed_pass(padded_x, spacing, 0, size_x + 2 * extra)
        padded_y = padded_1(along_x, "col", 1, width)
        along_y = holed_pass(padded_y, spacing, 1, size_y)
        smoother = depth_pass(along_y, spacing)
        padded_x = smoother if extra else None
        smoother = lax.slice_in_dim(smoother, extra, extra + size_x, axis=0)
        sums.append(moment_sums(current - smoother))
        current = smoother
    partial = jnp.sum(jnp.stack(sums), axis=-1)
    count_x = lax.axis_size("row") * size_x // SUB
    count_y = lax.axis_size("col") * size_y // SUB
    gathered = gather_partials(partial, ("row", "col"))
    rows, cols = lax.axis_size("row"), lax.axis_size("col")
    owner = np.zeros((count_x * count_y, rows * cols), np.float32)
    for r in range(rows):
        for c in range(cols):
            owner[(r * size_x // SUB) * count_y + c * size_y // SUB, r * cols + c] = 1.0
    summed = jnp.dot(
        jnp.asarray(owner), gathered, precision=lax.Precision.HIGHEST,
        preferred_element_type=jnp.float32,
    )
    table = jnp.transpose(summed.reshape(count_x, count_y, len(SPACINGS), 4), (2, 3, 0, 1))
    return (current, finish_table(table, planes))


def solution(mesh):
    placed = (P("row", "col", None),)
    return jax.shard_map(
        per_device,
        mesh=mesh,
        in_specs=placed,
        out_specs=(P("row", "col", None), P()),
        check_vma=False,
    )
```

```python
import jax
import jax.numpy as jnp
import numpy as np
from jax import lax
from jax.sharding import PartitionSpec as P

SUB = 256


SPLINE_TAPS = (0.0625, 0.25, 0.375, 0.25, 0.0625)
SPACINGS = (4, 8, 16)
EPSILON = 1e-06


def ring_pairs(count):
    forward = [(i, (i + 1) % count) for i in range(count)]
    backward = [(target, source) for source, target in forward]
    return forward, backward


def padded_1(block, axis, dim, width):
    count = lax.axis_size(axis)
    assert width <= block.shape[dim]
    forward, backward = ring_pairs(count)
    low = lax.ppermute(
        lax.slice_in_dim(block, block.shape[dim] - width, None, axis=dim), axis, forward
    )
    high = lax.ppermute(lax.slice_in_dim(block, 0, width, axis=dim), axis, backward)
    return jnp.concatenate([low, block, high], axis=dim)


def holed_pass(padded, spacing, axis_number, length_out):
    summed = SPLINE_TAPS[0] * lax.slice_in_dim(padded, 0, length_out, axis=axis_number)
    for tap_index in (1, 2, 3, 4):
        portion = lax.slice_in_dim(
            padded, tap_index * spacing, tap_index * spacing + length_out, axis=axis_number
        )
        summed = summed + SPLINE_TAPS[tap_index] * portion
    return summed


def depth_matrix(planes, spacing):
    matrix = np.zeros((planes, planes), np.float32)
    for tap_index in range(5):
        for i in range(planes):
            matrix[(i + (tap_index - 2) * spacing) % planes, i] += SPLINE_TAPS[tap_index]
    return matrix


def depth_pass(values_in, spacing):
    rows = values_in.shape[:-1]
    planes = values_in.shape[-1]
    flat = values_in.reshape(-1, planes)
    summed = jnp.dot(
        flat,
        jnp.asarray(depth_matrix(planes, spacing)),
        precision=lax.Precision.HIGHEST,
        preferred_element_type=jnp.float32,
    )
    return summed.reshape(*rows, planes)


def moment_sums(detail):
    square = detail * detail
    return jnp.stack(
        [
            jnp.sum(jnp.abs(detail), axis=(0, 1)),
            jnp.sum(square, axis=(0, 1)),
            jnp.sum(square * detail, axis=(0, 1)),
            jnp.sum(square * square, axis=(0, 1)),
        ]
    )


def finish_table(table, planes):
    means = table / jnp.float32(SUB * SUB * planes)
    second = means[:, 1:2]
    column = lax.broadcasted_iota(jnp.int32, means.shape, 1)
    ones = jnp.ones_like(means)
    scale = jnp.where(
        column == 2, (second + EPSILON) ** 1.5, jnp.where(column == 3, (second + EPSILON) ** 2, ones)
    )
    return means / scale


def gather_partials(partial, axes):
    count = 1
    for axis in axes:
        count *= lax.axis_size(axis)
    flat = partial.reshape(1, -1)
    sent = jnp.broadcast_to(flat, (count, flat.shape[1]))
    return lax.all_to_all(sent, axes, 0, 0, tiled=True)


def per_device(density):
    size_x, size_y, planes = density.shape
    assert SUB % size_x == 0 and SUB % size_y == 0
    sums = []
    current = density
    padded_x = None
    for scale, spacing in enumerate(SPACINGS):
        width = 2 * spacing
        if scale == 0:
            extra = 2 * SPACINGS[1]
            padded_y = padded_1(current, "col", 1, width)
            along_y = holed_pass(padded_y, spacing, 1, size_y)
            padded_x = padded_1(along_y, "row", 0, width + extra)
            along_x = holed_pass(padded_x, spacing, 0, size_x + 2 * extra)
            wide = depth_pass(along_x, spacing)
            padded_x = wide
            smoother = lax.slice_in_dim(wide, extra, extra + size_x, axis=0)
        else:
            if padded_x is None:
                padded_x = padded_1(current, "row", 0, width)
            along_x = holed_pass(padded_x, spacing, 0, size_x)
            padded_x = None
            padded_y = padded_1(along_x, "col", 1, width)
            along_y = holed_pass(padded_y, spacing, 1, size_y)
            smoother = depth_pass(along_y, spacing)
        sums.append(moment_sums(current - smoother))
        current = smoother
    partial = jnp.sum(jnp.stack(sums), axis=-1)
    count_x = lax.axis_size("row") * size_x // SUB
    count_y = lax.axis_size("col") * size_y // SUB
    gathered = gather_partials(partial, ("row", "col"))
    rows, cols = lax.axis_size("row"), lax.axis_size("col")
    owner = np.zeros((count_x * count_y, rows * cols), np.float32)
    for r in range(rows):
        for c in range(cols):
            owner[(r * size_x // SUB) * count_y + c * size_y // SUB, r * cols + c] = 1.0
    summed = jnp.dot(
        jnp.asarray(owner), gathered, precision=lax.Precision.HIGHEST,
        preferred_element_type=jnp.float32,
    )
    table = jnp.transpose(summed.reshape(count_x, count_y, len(SPACINGS), 4), (2, 3, 0, 1))
    return (current, finish_table(table, planes))


def solution(mesh):
    placed = (P("row", "col", None),)
    return jax.shard_map(
        per_device,
        mesh=mesh,
        in_specs=placed,
        out_specs=(P("row", "col", None), P()),
        check_vma=False,
    )
```

```python
import jax
import jax.numpy as jnp
import numpy as np
from jax import lax
from jax.sharding import PartitionSpec as P

SUB = 256


SPLINE_TAPS = (0.0625, 0.25, 0.375, 0.25, 0.0625)
SPACINGS = (4, 8, 16)
EPSILON = 1e-06


def ring_pairs(count):
    forward = [(i, (i + 1) % count) for i in range(count)]
    backward = [(target, source) for source, target in forward]
    return forward, backward


def padded_1(block, axis, dim, width):
    count = lax.axis_size(axis)
    assert width <= block.shape[dim]
    forward, backward = ring_pairs(count)
    low = lax.ppermute(
        lax.slice_in_dim(block, block.shape[dim] - width, None, axis=dim), axis, forward
    )
    high = lax.ppermute(lax.slice_in_dim(block, 0, width, axis=dim), axis, backward)
    return jnp.concatenate([low, block, high], axis=dim)


def holed_pass(padded, spacing, axis_number, length_out):
    summed = SPLINE_TAPS[0] * lax.slice_in_dim(padded, 0, length_out, axis=axis_number)
    for tap_index in (1, 2, 3, 4):
        portion = lax.slice_in_dim(
            padded, tap_index * spacing, tap_index * spacing + length_out, axis=axis_number
        )
        summed = summed + SPLINE_TAPS[tap_index] * portion
    return summed


def depth_matrix(planes, spacing):
    matrix = np.zeros((planes, planes), np.float32)
    for tap_index in range(5):
        for i in range(planes):
            matrix[(i + (tap_index - 2) * spacing) % planes, i] += SPLINE_TAPS[tap_index]
    return matrix


def depth_pass(values_in, spacing):
    rows = values_in.shape[:-1]
    planes = values_in.shape[-1]
    flat = values_in.reshape(-1, planes)
    summed = jnp.dot(
        flat,
        jnp.asarray(depth_matrix(planes, spacing)),
        precision=lax.Precision.HIGHEST,
        preferred_element_type=jnp.float32,
    )
    return summed.reshape(*rows, planes)


def moment_sums(detail):
    square = detail * detail
    return jnp.stack(
        [
            jnp.sum(jnp.abs(detail), axis=(0, 1)),
            jnp.sum(square, axis=(0, 1)),
            jnp.sum(square * detail, axis=(0, 1)),
            jnp.sum(square * square, axis=(0, 1)),
        ]
    )


def finish_table(table, planes):
    means = table / jnp.float32(SUB * SUB * planes)
    second = means[:, 1]
    third = means[:, 2] / (second + EPSILON) ** 1.5
    fourth = means[:, 3] / (second + EPSILON) ** 2
    return jnp.stack([means[:, 0], second, third, fourth], axis=1)


def gather_partials(partial, axes):
    count = 1
    for axis in axes:
        count *= lax.axis_size(axis)
    flat = partial.reshape(1, -1)
    sent = jnp.broadcast_to(flat, (count, flat.shape[1]))
    return lax.all_to_all(sent, axes, 0, 0, tiled=True)


def per_device(density):
    size_x, size_y, planes = density.shape
    assert SUB % size_x == 0 and SUB % size_y == 0
    sums = []
    current = density
    padded_x = None
    for scale, spacing in enumerate(SPACINGS):
        width = 2 * spacing
        if scale == 0:
            extra = 2 * SPACINGS[1]
            padded_y = padded_1(current, "col", 1, width)
            along_y = holed_pass(padded_y, spacing, 1, size_y)
            padded_x = padded_1(along_y, "row", 0, width + extra)
            along_x = holed_pass(padded_x, spacing, 0, size_x + 2 * extra)
            wide = depth_pass(along_x, spacing)
            padded_x = wide
            smoother = lax.slice_in_dim(wide, extra, extra + size_x, axis=0)
        else:
            if padded_x is None:
                padded_x = padded_1(current, "row", 0, width)
            along_x = holed_pass(padded_x, spacing, 0, size_x)
            padded_x = None
            padded_y = padded_1(along_x, "col", 1, width)
            along_y = holed_pass(padded_y, spacing, 1, size_y)
            smoother = depth_pass(along_y, spacing)
        sums.append(moment_sums(current - smoother))
        current = smoother
    partial = jnp.sum(jnp.stack(sums), axis=-1)
    count_x = lax.axis_size("row") * size_x // SUB
    count_y = lax.axis_size("col") * size_y // SUB
    gathered = gather_partials(partial, ("row", "col"))
    per_x = SUB // size_x
    per_y = SUB // size_y
    grouped = gathered.reshape(count_x, per_x, count_y, per_y, len(SPACINGS), 4)
    table = jnp.transpose(jnp.sum(grouped, axis=(1, 3)), (2, 3, 0, 1))
    return (current, finish_table(table, planes))


def solution(mesh):
    placed = (P("row", "col", None),)
    return jax.shard_map(
        per_device,
        mesh=mesh,
        in_specs=placed,
        out_specs=(P("row", "col", None), P()),
        check_vma=False,
    )
```

```python
import jax
import jax.numpy as jnp
import numpy as np
from jax import lax
from jax.sharding import PartitionSpec as P

SUB = 256


SPLINE_TAPS = (0.0625, 0.25, 0.375, 0.25, 0.0625)
SPACINGS = (4, 8, 16)
EPSILON = 1e-06


def ring_pairs(count):
    forward = [(i, (i + 1) % count) for i in range(count)]
    backward = [(target, source) for source, target in forward]
    return forward, backward


def padded_1(block, axis, dim, width):
    count = lax.axis_size(axis)
    assert width <= block.shape[dim]
    forward, backward = ring_pairs(count)
    low = lax.ppermute(
        lax.slice_in_dim(block, block.shape[dim] - width, None, axis=dim), axis, forward
    )
    high = lax.ppermute(lax.slice_in_dim(block, 0, width, axis=dim), axis, backward)
    return jnp.concatenate([low, block, high], axis=dim)


def holed_pass(padded, spacing, axis_number, length_out):
    summed = SPLINE_TAPS[0] * lax.slice_in_dim(padded, 0, length_out, axis=axis_number)
    for tap_index in (1, 2, 3, 4):
        portion = lax.slice_in_dim(
            padded, tap_index * spacing, tap_index * spacing + length_out, axis=axis_number
        )
        summed = summed + SPLINE_TAPS[tap_index] * portion
    return summed


def depth_matrix(planes, spacing):
    matrix = np.zeros((planes, planes), np.float32)
    for tap_index in range(5):
        for i in range(planes):
            matrix[(i + (tap_index - 2) * spacing) % planes, i] += SPLINE_TAPS[tap_index]
    return matrix


def depth_pass(values_in, spacing):
    rows = values_in.shape[:-1]
    planes = values_in.shape[-1]
    flat = values_in.reshape(-1, planes)
    high = lax.reduce_precision(flat, exponent_bits=8, mantissa_bits=7)
    rest = flat - high
    middle = lax.reduce_precision(rest, exponent_bits=8, mantissa_bits=7)
    low = rest - middle
    pieces = jnp.concatenate([high, middle, low], axis=1).astype(jnp.bfloat16)
    matrix = depth_matrix(planes, spacing)
    stacked = jnp.asarray(np.concatenate([matrix] * 3, axis=0), dtype=jnp.bfloat16)
    summed = jnp.dot(pieces, stacked, preferred_element_type=jnp.float32)
    return summed.reshape(*rows, planes)


def moment_sums(detail):
    square = detail * detail
    return jnp.stack(
        [
            jnp.sum(jnp.abs(detail), axis=(0, 1)),
            jnp.sum(square, axis=(0, 1)),
            jnp.sum(square * detail, axis=(0, 1)),
            jnp.sum(square * square, axis=(0, 1)),
        ]
    )


def finish_table(table, planes):
    means = table / jnp.float32(SUB * SUB * planes)
    second = means[:, 1]
    third = means[:, 2] / (second + EPSILON) ** 1.5
    fourth = means[:, 3] / (second + EPSILON) ** 2
    return jnp.stack([means[:, 0], second, third, fourth], axis=1)


def gather_partials(partial, axes):
    count = 1
    for axis in axes:
        count *= lax.axis_size(axis)
    flat = partial.reshape(1, -1)
    sent = jnp.broadcast_to(flat, (count, flat.shape[1]))
    return lax.all_to_all(sent, axes, 0, 0, tiled=True)


def per_device(density):
    size_x, size_y, planes = density.shape
    assert SUB % size_x == 0 and SUB % size_y == 0
    sums = []
    current = density
    padded_x = None
    for scale, spacing in enumerate(SPACINGS):
        width = 2 * spacing
        if scale == 0:
            extra = 2 * SPACINGS[1]
            padded_y = padded_1(current, "col", 1, width)
            along_y = holed_pass(padded_y, spacing, 1, size_y)
            padded_x = padded_1(along_y, "row", 0, width + extra)
            along_x = holed_pass(padded_x, spacing, 0, size_x + 2 * extra)
            wide = depth_pass(along_x, spacing)
            padded_x = wide
            smoother = lax.slice_in_dim(wide, extra, extra + size_x, axis=0)
        else:
            if padded_x is None:
                padded_x = padded_1(current, "row", 0, width)
            along_x = holed_pass(padded_x, spacing, 0, size_x)
            padded_x = None
            padded_y = padded_1(along_x, "col", 1, width)
            along_y = holed_pass(padded_y, spacing, 1, size_y)
            smoother = depth_pass(along_y, spacing)
        sums.append(moment_sums(current - smoother))
        current = smoother
    partial = jnp.sum(jnp.stack(sums), axis=-1)
    count_x = lax.axis_size("row") * size_x // SUB
    count_y = lax.axis_size("col") * size_y // SUB
    gathered = gather_partials(partial, ("row", "col"))
    per_x = SUB // size_x
    per_y = SUB // size_y
    grouped = gathered.reshape(count_x, per_x, count_y, per_y, len(SPACINGS), 4)
    table = jnp.transpose(jnp.sum(grouped, axis=(1, 3)), (2, 3, 0, 1))
    return (current, finish_table(table, planes))


def solution(mesh):
    placed = (P("row", "col", None),)
    return jax.shard_map(
        per_device,
        mesh=mesh,
        in_specs=placed,
        out_specs=(P("row", "col", None), P()),
        check_vma=False,
    )
```

```python
import jax
import jax.numpy as jnp
import numpy as np
from jax import lax
from jax.sharding import PartitionSpec as P

SUB = 256


SPLINE_TAPS = (0.0625, 0.25, 0.375, 0.25, 0.0625)
SPACINGS = (4, 8, 16)
EPSILON = 1e-06


def ring_pairs(count):
    forward = [(i, (i + 1) % count) for i in range(count)]
    backward = [(target, source) for source, target in forward]
    return forward, backward


def padded_1(block, axis, dim, width):
    count = lax.axis_size(axis)
    assert width <= block.shape[dim]
    forward, backward = ring_pairs(count)
    low = lax.ppermute(
        lax.slice_in_dim(block, block.shape[dim] - width, None, axis=dim), axis, forward
    )
    high = lax.ppermute(lax.slice_in_dim(block, 0, width, axis=dim), axis, backward)
    return jnp.concatenate([low, block, high], axis=dim)


def holed_pass(padded, spacing, axis_number, length_out):
    summed = SPLINE_TAPS[0] * lax.slice_in_dim(padded, 0, length_out, axis=axis_number)
    for tap_index in (1, 2, 3, 4):
        portion = lax.slice_in_dim(
            padded, tap_index * spacing, tap_index * spacing + length_out, axis=axis_number
        )
        summed = summed + SPLINE_TAPS[tap_index] * portion
    return summed


def depth_matrix(planes, spacing):
    matrix = np.zeros((planes, planes), np.float32)
    for tap_index in range(5):
        for i in range(planes):
            matrix[(i + (tap_index - 2) * spacing) % planes, i] += SPLINE_TAPS[tap_index]
    return matrix


def depth_pass(values_in, spacing):
    rows = values_in.shape[:-1]
    planes = values_in.shape[-1]
    flat = values_in.reshape(-1, planes)
    summed = jnp.dot(
        flat,
        jnp.asarray(depth_matrix(planes, spacing)),
        precision=lax.Precision.HIGHEST,
        preferred_element_type=jnp.float32,
    )
    return summed.reshape(*rows, planes)


def moment_sums(detail):
    square = detail * detail
    return jnp.stack(
        [
            jnp.sum(jnp.abs(detail), axis=(0, 1)),
            jnp.sum(square, axis=(0, 1)),
            jnp.sum(square * detail, axis=(0, 1)),
            jnp.sum(square * square, axis=(0, 1)),
        ]
    )


def finish_table(table, planes):
    means = table / jnp.float32(SUB * SUB * planes)
    second = means[:, 1]
    third = means[:, 2] / (second + EPSILON) ** 1.5
    fourth = means[:, 3] / (second + EPSILON) ** 2
    return jnp.stack([means[:, 0], second, third, fourth], axis=1)


def gather_partials(partial, axes):
    count = 1
    for axis in axes:
        count *= lax.axis_size(axis)
    flat = partial.reshape(1, -1)
    sent = jnp.broadcast_to(flat, (count, flat.shape[1]))
    return lax.all_to_all(sent, axes, 0, 0, tiled=True)


def per_device(density):
    size_x, size_y, planes = density.shape
    assert SUB % size_x == 0 and SUB % size_y == 0
    pairs = []
    current = density
    padded_x = None
    last = len(SPACINGS) - 1
    for scale, spacing in enumerate(SPACINGS):
        width = 2 * spacing
        if scale == 0:
            extra = 2 * SPACINGS[1]
            padded_y = padded_1(current, "col", 1, width)
            along_y = holed_pass(padded_y, spacing, 1, size_y)
            padded_x = padded_1(along_y, "row", 0, width + extra)
            along_x = holed_pass(padded_x, spacing, 0, size_x + 2 * extra)
            wide = depth_pass(along_x, spacing)
            padded_x = wide
            smoother = lax.slice_in_dim(wide, extra, extra + size_x, axis=0)
        else:
            if padded_x is None:
                padded_x = padded_1(current, "row", 0, width)
            along_x = holed_pass(padded_x, spacing, 0, size_x)
            padded_x = None
            padded_y = padded_1(along_x, "col", 1, width)
            along_y = holed_pass(padded_y, spacing, 1, size_y)
            smoother = depth_pass(along_y, spacing)
        if scale == last:
            held = lax.optimization_barrier(pairs)
            sums = [moment_sums(a - b) for a, b in held]
        pairs.append((current, smoother))
        current = smoother
    sums.append(moment_sums(pairs[-1][0] - pairs[-1][1]))
    partial = jnp.sum(jnp.stack(sums), axis=-1)
    count_x = lax.axis_size("row") * size_x // SUB
    count_y = lax.axis_size("col") * size_y // SUB
    gathered = gather_partials(partial, ("row", "col"))
    per_x = SUB // size_x
    per_y = SUB // size_y
    grouped = gathered.reshape(count_x, per_x, count_y, per_y, len(SPACINGS), 4)
    table = jnp.transpose(jnp.sum(grouped, axis=(1, 3)), (2, 3, 0, 1))
    return (current, finish_table(table, planes))


def solution(mesh):
    placed = (P("row", "col", None),)
    return jax.shard_map(
        per_device,
        mesh=mesh,
        in_specs=placed,
        out_specs=(P("row", "col", None), P()),
        check_vma=False,
    )
```

```python
import jax
import jax.numpy as jnp
import numpy as np
from jax import lax
from jax.sharding import PartitionSpec as P

SUB = 256


SPLINE_TAPS = (0.0625, 0.25, 0.375, 0.25, 0.0625)
SPACINGS = (4, 8, 16)
EPSILON = 1e-06


def ring_pairs(count):
    forward = [(i, (i + 1) % count) for i in range(count)]
    backward = [(target, source) for source, target in forward]
    return forward, backward


def padded_1(block, axis, dim, width):
    count = lax.axis_size(axis)
    assert width <= block.shape[dim]
    forward, backward = ring_pairs(count)
    low = lax.ppermute(
        lax.slice_in_dim(block, block.shape[dim] - width, None, axis=dim), axis, forward
    )
    high = lax.ppermute(lax.slice_in_dim(block, 0, width, axis=dim), axis, backward)
    return jnp.concatenate([low, block, high], axis=dim)


def holed_pass(padded, spacing, axis_number, length_out):
    summed = SPLINE_TAPS[0] * lax.slice_in_dim(padded, 0, length_out, axis=axis_number)
    for tap_index in (1, 2, 3, 4):
        portion = lax.slice_in_dim(
            padded, tap_index * spacing, tap_index * spacing + length_out, axis=axis_number
        )
        summed = summed + SPLINE_TAPS[tap_index] * portion
    return summed


def depth_matrix(planes, spacing):
    matrix = np.zeros((planes, planes), np.float32)
    for tap_index in range(5):
        for i in range(planes):
            matrix[(i + (tap_index - 2) * spacing) % planes, i] += SPLINE_TAPS[tap_index]
    return matrix


def depth_pass(values_in, matrix):
    rows = values_in.shape[:-1]
    planes = values_in.shape[-1]
    flat = values_in.reshape(-1, planes)
    summed = jnp.dot(
        flat,
        jnp.asarray(matrix),
        precision=lax.Precision.HIGHEST,
        preferred_element_type=jnp.float32,
    )
    return summed.reshape(*rows, matrix.shape[1])


def moment_sums(detail):
    square = detail * detail
    return jnp.stack(
        [
            jnp.sum(jnp.abs(detail), axis=(0, 1)),
            jnp.sum(square, axis=(0, 1)),
            jnp.sum(square * detail, axis=(0, 1)),
            jnp.sum(square * square, axis=(0, 1)),
        ]
    )


def finish_table(table, planes):
    means = table / jnp.float32(SUB * SUB * planes)
    second = means[:, 1]
    third = means[:, 2] / (second + EPSILON) ** 1.5
    fourth = means[:, 3] / (second + EPSILON) ** 2
    return jnp.stack([means[:, 0], second, third, fourth], axis=1)


def gather_partials(partial, axes):
    count = 1
    for axis in axes:
        count *= lax.axis_size(axis)
    flat = partial.reshape(1, -1)
    sent = jnp.broadcast_to(flat, (count, flat.shape[1]))
    return lax.all_to_all(sent, axes, 0, 0, tiled=True)


def per_device(density):
    size_x, size_y, planes = density.shape
    assert SUB % size_x == 0 and SUB % size_y == 0
    assert len(SPACINGS) == 3
    first, second, third = SPACINGS
    matrix_1 = depth_matrix(planes, first)
    matrix_2 = depth_matrix(planes, second)
    matrix_3 = depth_matrix(planes, third)
    extra = 2 * second
    padded_y = padded_1(density, "col", 1, 2 * first)
    along_y = holed_pass(padded_y, first, 1, size_y)
    padded_x = padded_1(along_y, "row", 0, 2 * first + extra)
    along_x = holed_pass(padded_x, first, 0, size_x + 2 * extra)
    both = depth_pass(along_x, np.concatenate([matrix_1, matrix_1 @ matrix_2], axis=1))
    smooth_1 = lax.slice_in_dim(both[..., :planes], extra, extra + size_x, axis=0)
    ahead_2 = both[..., planes:]
    along_x = holed_pass(ahead_2, second, 0, size_x)
    padded_y = padded_1(along_x, "col", 1, 2 * second)
    smooth_2 = holed_pass(padded_y, second, 1, size_y)
    ahead_3 = depth_pass(smooth_2, matrix_3)
    padded_x = padded_1(ahead_3, "row", 0, 2 * third)
    along_x = holed_pass(padded_x, third, 0, size_x)
    padded_y = padded_1(along_x, "col", 1, 2 * third)
    smooth_3 = holed_pass(padded_y, third, 1, size_y)
    current = smooth_3
    held = lax.optimization_barrier(((density, smooth_1), (smooth_1, smooth_2)))
    sums = [moment_sums(a - b) for a, b in held]
    sums.append(moment_sums(smooth_2 - smooth_3))
    partial = jnp.sum(jnp.stack(sums), axis=-1)
    count_x = lax.axis_size("row") * size_x // SUB
    count_y = lax.axis_size("col") * size_y // SUB
    gathered = gather_partials(partial, ("row", "col"))
    per_x = SUB // size_x
    per_y = SUB // size_y
    grouped = gathered.reshape(count_x, per_x, count_y, per_y, len(SPACINGS), 4)
    table = jnp.transpose(jnp.sum(grouped, axis=(1, 3)), (2, 3, 0, 1))
    return (current, finish_table(table, planes))


def solution(mesh):
    placed = (P("row", "col", None),)
    step = jax.shard_map(
        per_device,
        mesh=mesh,
        in_specs=placed,
        out_specs=(P("row", "col", None), P()),
        check_vma=False,
    )
    return step
```

```python
import jax
import jax.numpy as jnp
import numpy as np
from jax import lax
from jax.sharding import PartitionSpec as P

SUB = 256


SPLINE_TAPS = (0.0625, 0.25, 0.375, 0.25, 0.0625)
SPACINGS = (4, 8, 16)
EPSILON = 1e-06


def ring_pairs(count):
    forward = [(i, (i + 1) % count) for i in range(count)]
    backward = [(target, source) for source, target in forward]
    return forward, backward


def padded_1(block, axis, dim, width):
    count = lax.axis_size(axis)
    assert width <= block.shape[dim]
    forward, backward = ring_pairs(count)
    low = lax.ppermute(
        lax.slice_in_dim(block, block.shape[dim] - width, None, axis=dim), axis, forward
    )
    high = lax.ppermute(lax.slice_in_dim(block, 0, width, axis=dim), axis, backward)
    return jnp.concatenate([low, block, high], axis=dim)


def holed_pass(padded, spacing, axis_number, length_out):
    summed = SPLINE_TAPS[0] * lax.slice_in_dim(padded, 0, length_out, axis=axis_number)
    for tap_index in (1, 2, 3, 4):
        portion = lax.slice_in_dim(
            padded, tap_index * spacing, tap_index * spacing + length_out, axis=axis_number
        )
        summed = summed + SPLINE_TAPS[tap_index] * portion
    return summed


def depth_matrix(planes, spacing):
    matrix = np.zeros((planes, planes), np.float32)
    for tap_index in range(5):
        for i in range(planes):
            matrix[(i + (tap_index - 2) * spacing) % planes, i] += SPLINE_TAPS[tap_index]
    return matrix


def depth_pass(values_in, matrix):
    rows = values_in.shape[:-1]
    planes = values_in.shape[-1]
    flat = values_in.reshape(-1, planes)
    summed = jnp.dot(
        flat,
        jnp.asarray(matrix),
        precision=lax.Precision.HIGHEST,
        preferred_element_type=jnp.float32,
    )
    return summed.reshape(*rows, matrix.shape[1])


def moment_sums(detail):
    square = detail * detail
    return jnp.stack(
        [
            jnp.sum(jnp.abs(detail), axis=(0, 1)),
            jnp.sum(square, axis=(0, 1)),
            jnp.sum(square * detail, axis=(0, 1)),
            jnp.sum(square * square, axis=(0, 1)),
        ]
    )


def finish_table(table, planes):
    means = table / jnp.float32(SUB * SUB * planes)
    second = means[:, 1]
    third = means[:, 2] / (second + EPSILON) ** 1.5
    fourth = means[:, 3] / (second + EPSILON) ** 2
    return jnp.stack([means[:, 0], second, third, fourth], axis=1)


def gather_partials(partial, axes):
    count = 1
    for axis in axes:
        count *= lax.axis_size(axis)
    flat = partial.reshape(1, -1)
    sent = jnp.broadcast_to(flat, (count, flat.shape[1]))
    return lax.all_to_all(sent, axes, 0, 0, tiled=True)


def per_device(density):
    size_x, size_y, planes = density.shape
    assert SUB % size_x == 0 and SUB % size_y == 0
    assert len(SPACINGS) == 3
    first, second, third = SPACINGS
    matrix_1 = depth_matrix(planes, first)
    matrix_2 = depth_matrix(planes, second)
    matrix_3 = depth_matrix(planes, third)
    extra = 2 * second
    padded_y = padded_1(density, "col", 1, 2 * first)
    along_y = holed_pass(padded_y, first, 1, size_y)
    padded_x = padded_1(along_y, "row", 0, 2 * first + extra)
    along_x = holed_pass(padded_x, first, 0, size_x + 2 * extra)
    ahead_2 = depth_pass(along_x, matrix_1 @ matrix_2)
    smooth_1 = depth_pass(lax.slice_in_dim(along_x, extra, extra + size_x, axis=0), matrix_1)
    along_x = holed_pass(ahead_2, second, 0, size_x)
    padded_y = padded_1(along_x, "col", 1, 2 * second)
    smooth_2 = holed_pass(padded_y, second, 1, size_y)
    ahead_3 = depth_pass(smooth_2, matrix_3)
    padded_x = padded_1(ahead_3, "row", 0, 2 * third)
    along_x = holed_pass(padded_x, third, 0, size_x)
    padded_y = padded_1(along_x, "col", 1, 2 * third)
    smooth_3 = holed_pass(padded_y, third, 1, size_y)
    current = smooth_3
    held = lax.optimization_barrier(((density, smooth_1), (smooth_1, smooth_2)))
    sums = [moment_sums(a - b) for a, b in held]
    sums.append(moment_sums(smooth_2 - smooth_3))
    partial = jnp.sum(jnp.stack(sums), axis=-1)
    count_x = lax.axis_size("row") * size_x // SUB
    count_y = lax.axis_size("col") * size_y // SUB
    gathered = gather_partials(partial, ("row", "col"))
    per_x = SUB // size_x
    per_y = SUB // size_y
    grouped = gathered.reshape(count_x, per_x, count_y, per_y, len(SPACINGS), 4)
    table = jnp.transpose(jnp.sum(grouped, axis=(1, 3)), (2, 3, 0, 1))
    return (current, finish_table(table, planes))


def solution(mesh):
    placed = (P("row", "col", None),)
    step = jax.shard_map(
        per_device,
        mesh=mesh,
        in_specs=placed,
        out_specs=(P("row", "col", None), P()),
        check_vma=False,
    )
    return step
```

```python
import jax
import jax.numpy as jnp
import numpy as np
from jax import lax
from jax.sharding import PartitionSpec as P

SUB = 256


SPLINE_TAPS = (0.0625, 0.25, 0.375, 0.25, 0.0625)
SPACINGS = (4, 8, 16)
EPSILON = 1e-06


def ring_pairs(count):
    forward = [(i, (i + 1) % count) for i in range(count)]
    backward = [(target, source) for source, target in forward]
    return forward, backward


def padded_1(block, axis, dim, width):
    count = lax.axis_size(axis)
    assert width <= block.shape[dim]
    forward, backward = ring_pairs(count)
    low = lax.ppermute(
        lax.slice_in_dim(block, block.shape[dim] - width, None, axis=dim), axis, forward
    )
    high = lax.ppermute(lax.slice_in_dim(block, 0, width, axis=dim), axis, backward)
    return jnp.concatenate([low, block, high], axis=dim)


def holed_pass(padded, spacing, axis_number, length_out):
    summed = SPLINE_TAPS[0] * lax.slice_in_dim(padded, 0, length_out, axis=axis_number)
    for tap_index in (1, 2, 3, 4):
        portion = lax.slice_in_dim(
            padded, tap_index * spacing, tap_index * spacing + length_out, axis=axis_number
        )
        summed = summed + SPLINE_TAPS[tap_index] * portion
    return summed


def depth_matrix(planes, spacing):
    matrix = np.zeros((planes, planes), np.float32)
    for tap_index in range(5):
        for i in range(planes):
            matrix[(i + (tap_index - 2) * spacing) % planes, i] += SPLINE_TAPS[tap_index]
    return matrix


def composed_matrix(planes, spacing_a, spacing_b):
    source = lax.broadcasted_iota(jnp.int32, (planes, planes), 0)
    target = lax.broadcasted_iota(jnp.int32, (planes, planes), 1)
    zero = lax.convert_element_type(lax.axis_index("row"), jnp.float32) * 0.0
    matrix = jnp.zeros((planes, planes), jnp.float32) + zero
    for tap_a in range(5):
        for tap_b in range(5):
            shift = (tap_a - 2) * spacing_a + (tap_b - 2) * spacing_b
            weight = jnp.float32(SPLINE_TAPS[tap_a] * SPLINE_TAPS[tap_b])
            hit = (source - target - shift) % planes == 0
            matrix = matrix + jnp.where(hit, weight, jnp.float32(0.0))
    return matrix


def depth_pass(values_in, matrix):
    rows = values_in.shape[:-1]
    planes = values_in.shape[-1]
    flat = values_in.reshape(-1, planes)
    summed = jnp.dot(
        flat,
        matrix if isinstance(matrix, jax.Array) else jnp.asarray(matrix),
        precision=lax.Precision.HIGHEST,
        preferred_element_type=jnp.float32,
    )
    return summed.reshape(*rows, matrix.shape[1])


def moment_sums(detail):
    square = detail * detail
    return jnp.stack(
        [
            jnp.sum(jnp.abs(detail), axis=(0, 1)),
            jnp.sum(square, axis=(0, 1)),
            jnp.sum(square * detail, axis=(0, 1)),
            jnp.sum(square * square, axis=(0, 1)),
        ]
    )


def finish_table(table, planes):
    means = table / jnp.float32(SUB * SUB * planes)
    second = means[:, 1]
    third = means[:, 2] / (second + EPSILON) ** 1.5
    fourth = means[:, 3] / (second + EPSILON) ** 2
    return jnp.stack([means[:, 0], second, third, fourth], axis=1)


def gather_partials(partial, axes):
    count = 1
    for axis in axes:
        count *= lax.axis_size(axis)
    flat = partial.reshape(1, -1)
    sent = jnp.broadcast_to(flat, (count, flat.shape[1]))
    return lax.all_to_all(sent, axes, 0, 0, tiled=True)


def per_device(density):
    size_x, size_y, planes = density.shape
    assert SUB % size_x == 0 and SUB % size_y == 0
    assert len(SPACINGS) == 3
    first, second, third = SPACINGS
    matrix_1 = depth_matrix(planes, first)
    matrix_2 = depth_matrix(planes, second)
    matrix_3 = depth_matrix(planes, third)
    extra = 2 * second
    padded_y = padded_1(density, "col", 1, 2 * first)
    along_y = holed_pass(padded_y, first, 1, size_y)
    padded_x = padded_1(along_y, "row", 0, 2 * first + extra)
    along_x = holed_pass(padded_x, first, 0, size_x + 2 * extra)
    ahead_2 = depth_pass(along_x, composed_matrix(planes, first, second))
    smooth_1 = depth_pass(lax.slice_in_dim(along_x, extra, extra + size_x, axis=0), matrix_1)
    along_x = holed_pass(ahead_2, second, 0, size_x)
    padded_y = padded_1(along_x, "col", 1, 2 * second)
    smooth_2 = holed_pass(padded_y, second, 1, size_y)
    ahead_3 = depth_pass(smooth_2, matrix_3)
    padded_x = padded_1(ahead_3, "row", 0, 2 * third)
    along_x = holed_pass(padded_x, third, 0, size_x)
    padded_y = padded_1(along_x, "col", 1, 2 * third)
    smooth_3 = holed_pass(padded_y, third, 1, size_y)
    current = smooth_3
    held = lax.optimization_barrier(((density, smooth_1), (smooth_1, smooth_2)))
    sums = [moment_sums(a - b) for a, b in held]
    sums.append(moment_sums(smooth_2 - smooth_3))
    partial = jnp.sum(jnp.stack(sums), axis=-1)
    count_x = lax.axis_size("row") * size_x // SUB
    count_y = lax.axis_size("col") * size_y // SUB
    gathered = gather_partials(partial, ("row", "col"))
    per_x = SUB // size_x
    per_y = SUB // size_y
    grouped = gathered.reshape(count_x, per_x, count_y, per_y, len(SPACINGS), 4)
    table = jnp.transpose(jnp.sum(grouped, axis=(1, 3)), (2, 3, 0, 1))
    return (current, finish_table(table, planes))


def solution(mesh):
    placed = (P("row", "col", None),)
    step = jax.shard_map(
        per_device,
        mesh=mesh,
        in_specs=placed,
        out_specs=(P("row", "col", None), P()),
        check_vma=False,
    )
    return step
```

```python
import jax
import jax.numpy as jnp
import numpy as np
from jax import lax
from jax.sharding import PartitionSpec as P

SUB = 256


SPLINE_TAPS = (0.0625, 0.25, 0.375, 0.25, 0.0625)
SPACINGS = (4, 8, 16)
EPSILON = 1e-06


def ring_pairs(count):
    forward = [(i, (i + 1) % count) for i in range(count)]
    backward = [(target, source) for source, target in forward]
    return forward, backward


def padded_1(block, axis, dim, width):
    count = lax.axis_size(axis)
    assert width <= block.shape[dim]
    forward, backward = ring_pairs(count)
    low = lax.ppermute(
        lax.slice_in_dim(block, block.shape[dim] - width, None, axis=dim), axis, forward
    )
    high = lax.ppermute(lax.slice_in_dim(block, 0, width, axis=dim), axis, backward)
    return jnp.concatenate([low, block, high], axis=dim)


def holed_pass(padded, spacing, axis_number, length_out):
    summed = SPLINE_TAPS[0] * lax.slice_in_dim(padded, 0, length_out, axis=axis_number)
    for tap_index in (1, 2, 3, 4):
        portion = lax.slice_in_dim(
            padded, tap_index * spacing, tap_index * spacing + length_out, axis=axis_number
        )
        summed = summed + SPLINE_TAPS[tap_index] * portion
    return summed


def depth_matrix(planes, spacing):
    matrix = np.zeros((planes, planes), np.float32)
    for tap_index in range(5):
        for i in range(planes):
            matrix[(i + (tap_index - 2) * spacing) % planes, i] += SPLINE_TAPS[tap_index]
    return matrix


def depth_pass(values_in, matrix):
    rows = values_in.shape[:-1]
    planes = values_in.shape[-1]
    flat = values_in.reshape(-1, planes)
    summed = jnp.dot(
        flat,
        jnp.asarray(matrix),
        precision=lax.Precision.HIGHEST,
        preferred_element_type=jnp.float32,
    )
    return summed.reshape(*rows, matrix.shape[1])


def moment_sums(detail):
    square = detail * detail
    return jnp.stack(
        [
            jnp.sum(jnp.abs(detail), axis=(0, 1)),
            jnp.sum(square, axis=(0, 1)),
            jnp.sum(square * detail, axis=(0, 1)),
            jnp.sum(square * square, axis=(0, 1)),
        ]
    )


def finish_table(table, planes):
    means = table / jnp.float32(SUB * SUB * planes)
    second = means[:, 1]
    third = means[:, 2] / (second + EPSILON) ** 1.5
    fourth = means[:, 3] / (second + EPSILON) ** 2
    return jnp.stack([means[:, 0], second, third, fourth], axis=1)


def gather_partials(partial, axes):
    count = 1
    for axis in axes:
        count *= lax.axis_size(axis)
    flat = partial.reshape(1, -1)
    sent = jnp.broadcast_to(flat, (count, flat.shape[1]))
    return lax.all_to_all(sent, axes, 0, 0, tiled=True)


def per_device(density):
    size_x, size_y, planes = density.shape
    assert SUB % size_x == 0 and SUB % size_y == 0
    assert len(SPACINGS) == 3
    first, second, third = SPACINGS
    matrix_1 = depth_matrix(planes, first)
    matrix_2 = depth_matrix(planes, second)
    matrix_3 = depth_matrix(planes, third)
    extra = 2 * second
    padded_y = padded_1(density, "col", 1, 2 * first)
    along_y = holed_pass(padded_y, first, 1, size_y)
    padded_x = padded_1(along_y, "row", 0, 2 * first + extra)
    along_x = holed_pass(padded_x, first, 0, size_x + 2 * extra)
    ahead_2 = depth_pass(along_x, matrix_1 @ matrix_2)
    smooth_1 = depth_pass(lax.slice_in_dim(along_x, extra, extra + size_x, axis=0), matrix_1)
    along_x = holed_pass(ahead_2, second, 0, size_x)
    width = 2 * second
    assert width <= size_y
    forward, backward = ring_pairs(lax.axis_size("col"))
    low = lax.ppermute(along_x[:, size_y - width :], "col", forward)
    high = lax.ppermute(along_x[:, :width], "col", backward)
    smooth_2 = holed_pass(jnp.concatenate([low, along_x, high], axis=1), second, 1, size_y)
    ahead_pieces = [depth_pass(piece, matrix_3) for piece in (low, along_x, high)]
    ahead_3 = holed_pass(jnp.concatenate(ahead_pieces, axis=1), second, 1, size_y)
    padded_x = padded_1(ahead_3, "row", 0, 2 * third)
    along_x = holed_pass(padded_x, third, 0, size_x)
    padded_y = padded_1(along_x, "col", 1, 2 * third)
    smooth_3 = holed_pass(padded_y, third, 1, size_y)
    current = smooth_3
    held = lax.optimization_barrier(((density, smooth_1), (smooth_1, smooth_2)))
    sums = [moment_sums(a - b) for a, b in held]
    sums.append(moment_sums(smooth_2 - smooth_3))
    partial = jnp.sum(jnp.stack(sums), axis=-1)
    count_x = lax.axis_size("row") * size_x // SUB
    count_y = lax.axis_size("col") * size_y // SUB
    gathered = gather_partials(partial, ("row", "col"))
    per_x = SUB // size_x
    per_y = SUB // size_y
    grouped = gathered.reshape(count_x, per_x, count_y, per_y, len(SPACINGS), 4)
    table = jnp.transpose(jnp.sum(grouped, axis=(1, 3)), (2, 3, 0, 1))
    return (current, finish_table(table, planes))


def solution(mesh):
    placed = (P("row", "col", None),)
    step = jax.shard_map(
        per_device,
        mesh=mesh,
        in_specs=placed,
        out_specs=(P("row", "col", None), P()),
        check_vma=False,
    )
    return step
```

```python
import jax
import jax.numpy as jnp
import numpy as np
from jax import lax
from jax.sharding import PartitionSpec as P

SUB = 256


SPLINE_TAPS = (0.0625, 0.25, 0.375, 0.25, 0.0625)
SPACINGS = (4, 8, 16)
EPSILON = 1e-06


def ring_pairs(count):
    forward = [(i, (i + 1) % count) for i in range(count)]
    backward = [(target, source) for source, target in forward]
    return forward, backward


def padded_1(block, axis, dim, width):
    count = lax.axis_size(axis)
    assert width <= block.shape[dim]
    forward, backward = ring_pairs(count)
    low = lax.ppermute(
        lax.slice_in_dim(block, block.shape[dim] - width, None, axis=dim), axis, forward
    )
    high = lax.ppermute(lax.slice_in_dim(block, 0, width, axis=dim), axis, backward)
    return jnp.concatenate([low, block, high], axis=dim)


def holed_pass(padded, spacing, axis_number, length_out):
    summed = SPLINE_TAPS[0] * lax.slice_in_dim(padded, 0, length_out, axis=axis_number)
    for tap_index in (1, 2, 3, 4):
        portion = lax.slice_in_dim(
            padded, tap_index * spacing, tap_index * spacing + length_out, axis=axis_number
        )
        summed = summed + SPLINE_TAPS[tap_index] * portion
    return summed


def depth_matrix(planes, spacing):
    matrix = np.zeros((planes, planes), np.float32)
    for tap_index in range(5):
        for i in range(planes):
            matrix[(i + (tap_index - 2) * spacing) % planes, i] += SPLINE_TAPS[tap_index]
    return matrix


def depth_pass(values_in, matrix):
    rows = values_in.shape[:-1]
    planes = values_in.shape[-1]
    flat = values_in.reshape(-1, planes)
    summed = jnp.dot(
        flat,
        jnp.asarray(matrix),
        precision=lax.Precision.HIGHEST,
        preferred_element_type=jnp.float32,
    )
    return summed.reshape(*rows, matrix.shape[1])


def moment_sums(detail):
    square = detail * detail
    return jnp.stack(
        [
            jnp.sum(jnp.abs(detail), axis=(0, 1)),
            jnp.sum(square, axis=(0, 1)),
            jnp.sum(square * detail, axis=(0, 1)),
            jnp.sum(square * square, axis=(0, 1)),
        ]
    )


def finish_table(table, planes):
    means = table / jnp.float32(SUB * SUB * planes)
    second = means[:, 1]
    third = means[:, 2] / (second + EPSILON) ** 1.5
    fourth = means[:, 3] / (second + EPSILON) ** 2
    return jnp.stack([means[:, 0], second, third, fourth], axis=1)


def gather_partials(partial, axes):
    count = 1
    for axis in axes:
        count *= lax.axis_size(axis)
    flat = partial.reshape(1, -1)
    sent = jnp.broadcast_to(flat, (count, flat.shape[1]))
    return lax.all_to_all(sent, axes, 0, 0, tiled=True)


def per_device(density):
    size_x, size_y, planes = density.shape
    assert SUB % size_x == 0 and SUB % size_y == 0
    assert len(SPACINGS) == 3
    first, second, third = SPACINGS
    matrix_1 = depth_matrix(planes, first)
    matrix_2 = depth_matrix(planes, second)
    matrix_3 = depth_matrix(planes, third)
    extra = 2 * second
    padded_y = padded_1(density, "col", 1, 2 * first)
    along_y = holed_pass(padded_y, first, 1, size_y)
    padded_x = padded_1(along_y, "row", 0, 2 * first + extra)
    along_x = holed_pass(padded_x, first, 0, size_x + 2 * extra)
    smooth_1 = depth_pass(lax.slice_in_dim(along_x, extra, extra + size_x, axis=0), matrix_1)
    along_x = depth_pass(holed_pass(along_x, second, 0, size_x), matrix_1 @ matrix_2)
    padded_y = padded_1(along_x, "col", 1, 2 * second)
    smooth_2 = holed_pass(padded_y, second, 1, size_y)
    ahead_3 = depth_pass(smooth_2, matrix_3)
    padded_x = padded_1(ahead_3, "row", 0, 2 * third)
    along_x = holed_pass(padded_x, third, 0, size_x)
    padded_y = padded_1(along_x, "col", 1, 2 * third)
    smooth_3 = holed_pass(padded_y, third, 1, size_y)
    current = smooth_3
    held = lax.optimization_barrier(((density, smooth_1), (smooth_1, smooth_2)))
    sums = [moment_sums(a - b) for a, b in held]
    sums.append(moment_sums(smooth_2 - smooth_3))
    partial = jnp.sum(jnp.stack(sums), axis=-1)
    count_x = lax.axis_size("row") * size_x // SUB
    count_y = lax.axis_size("col") * size_y // SUB
    gathered = gather_partials(partial, ("row", "col"))
    per_x = SUB // size_x
    per_y = SUB // size_y
    grouped = gathered.reshape(count_x, per_x, count_y, per_y, len(SPACINGS), 4)
    table = jnp.transpose(jnp.sum(grouped, axis=(1, 3)), (2, 3, 0, 1))
    return (current, finish_table(table, planes))


def solution(mesh):
    placed = (P("row", "col", None),)
    step = jax.shard_map(
        per_device,
        mesh=mesh,
        in_specs=placed,
        out_specs=(P("row", "col", None), P()),
        check_vma=False,
    )
    return step
```

```python
import jax
import jax.numpy as jnp
import numpy as np
from jax import lax
from jax.sharding import PartitionSpec as P

SUB = 256


SPLINE_TAPS = (0.0625, 0.25, 0.375, 0.25, 0.0625)
SPACINGS = (4, 8, 16)
EPSILON = 1e-06


def ring_pairs(count):
    forward = [(i, (i + 1) % count) for i in range(count)]
    backward = [(target, source) for source, target in forward]
    return forward, backward


def padded_1(block, axis, dim, width):
    count = lax.axis_size(axis)
    assert width <= block.shape[dim]
    forward, backward = ring_pairs(count)
    low = lax.ppermute(
        lax.slice_in_dim(block, block.shape[dim] - width, None, axis=dim), axis, forward
    )
    high = lax.ppermute(lax.slice_in_dim(block, 0, width, axis=dim), axis, backward)
    return jnp.concatenate([low, block, high], axis=dim)


def holed_pass(padded, spacing, axis_number, length_out):
    summed = SPLINE_TAPS[0] * lax.slice_in_dim(padded, 0, length_out, axis=axis_number)
    for tap_index in (1, 2, 3, 4):
        portion = lax.slice_in_dim(
            padded, tap_index * spacing, tap_index * spacing + length_out, axis=axis_number
        )
        summed = summed + SPLINE_TAPS[tap_index] * portion
    return summed


def depth_matrix(planes, spacing):
    matrix = np.zeros((planes, planes), np.float32)
    for tap_index in range(5):
        for i in range(planes):
            matrix[(i + (tap_index - 2) * spacing) % planes, i] += SPLINE_TAPS[tap_index]
    return matrix


def depth_pass(values_in, matrix):
    rows = values_in.shape[:-1]
    planes = values_in.shape[-1]
    flat = values_in.reshape(-1, planes)
    summed = jnp.dot(
        flat,
        jnp.asarray(matrix),
        precision=lax.Precision.HIGH,
        preferred_element_type=jnp.float32,
    )
    return summed.reshape(*rows, matrix.shape[1])


def moment_sums(detail):
    square = detail * detail
    return jnp.stack(
        [
            jnp.sum(jnp.abs(detail), axis=(0, 1)),
            jnp.sum(square, axis=(0, 1)),
            jnp.sum(square * detail, axis=(0, 1)),
            jnp.sum(square * square, axis=(0, 1)),
        ]
    )


def finish_table(table, planes):
    means = table / jnp.float32(SUB * SUB * planes)
    second = means[:, 1]
    third = means[:, 2] / (second + EPSILON) ** 1.5
    fourth = means[:, 3] / (second + EPSILON) ** 2
    return jnp.stack([means[:, 0], second, third, fourth], axis=1)


def gather_partials(partial, axes):
    count = 1
    for axis in axes:
        count *= lax.axis_size(axis)
    flat = partial.reshape(1, -1)
    sent = jnp.broadcast_to(flat, (count, flat.shape[1]))
    return lax.all_to_all(sent, axes, 0, 0, tiled=True)


def per_device(density):
    size_x, size_y, planes = density.shape
    assert SUB % size_x == 0 and SUB % size_y == 0
    assert len(SPACINGS) == 3
    first, second, third = SPACINGS
    matrix_1 = depth_matrix(planes, first)
    matrix_2 = depth_matrix(planes, second)
    matrix_3 = depth_matrix(planes, third)
    extra = 2 * second
    padded_y = padded_1(density, "col", 1, 2 * first)
    along_y = holed_pass(padded_y, first, 1, size_y)
    padded_x = padded_1(along_y, "row", 0, 2 * first + extra)
    along_x = holed_pass(padded_x, first, 0, size_x + 2 * extra)
    smooth_1 = depth_pass(lax.slice_in_dim(along_x, extra, extra + size_x, axis=0), matrix_1)
    along_x = depth_pass(holed_pass(along_x, second, 0, size_x), matrix_1 @ matrix_2)
    padded_y = padded_1(along_x, "col", 1, 2 * second)
    smooth_2 = holed_pass(padded_y, second, 1, size_y)
    ahead_3 = depth_pass(smooth_2, matrix_3)
    padded_x = padded_1(ahead_3, "row", 0, 2 * third)
    along_x = holed_pass(padded_x, third, 0, size_x)
    padded_y = padded_1(along_x, "col", 1, 2 * third)
    smooth_3 = holed_pass(padded_y, third, 1, size_y)
    current = smooth_3
    held = lax.optimization_barrier(((density, smooth_1), (smooth_1, smooth_2)))
    sums = [moment_sums(a - b) for a, b in held]
    sums.append(moment_sums(smooth_2 - smooth_3))
    partial = jnp.sum(jnp.stack(sums), axis=-1)
    count_x = lax.axis_size("row") * size_x // SUB
    count_y = lax.axis_size("col") * size_y // SUB
    gathered = gather_partials(partial, ("row", "col"))
    per_x = SUB // size_x
    per_y = SUB // size_y
    grouped = gathered.reshape(count_x, per_x, count_y, per_y, len(SPACINGS), 4)
    table = jnp.transpose(jnp.sum(grouped, axis=(1, 3)), (2, 3, 0, 1))
    return (current, finish_table(table, planes))


def solution(mesh):
    placed = (P("row", "col", None),)
    step = jax.shard_map(
        per_device,
        mesh=mesh,
        in_specs=placed,
        out_specs=(P("row", "col", None), P()),
        check_vma=False,
    )
    return step
```

```python
import jax
import jax.numpy as jnp
import numpy as np
from jax import lax
from jax.sharding import PartitionSpec as P

SUB = 256


SPLINE_TAPS = (0.0625, 0.25, 0.375, 0.25, 0.0625)
SPACINGS = (4, 8, 16)
EPSILON = 1e-06


def ring_pairs(count):
    forward = [(i, (i + 1) % count) for i in range(count)]
    backward = [(target, source) for source, target in forward]
    return forward, backward


def padded_1(block, axis, dim, width):
    count = lax.axis_size(axis)
    assert width <= block.shape[dim]
    forward, backward = ring_pairs(count)
    low = lax.ppermute(
        lax.slice_in_dim(block, block.shape[dim] - width, None, axis=dim), axis, forward
    )
    high = lax.ppermute(lax.slice_in_dim(block, 0, width, axis=dim), axis, backward)
    return jnp.concatenate([low, block, high], axis=dim)


def holed_pass(padded, spacing, axis_number, length_out):
    summed = SPLINE_TAPS[0] * lax.slice_in_dim(padded, 0, length_out, axis=axis_number)
    for tap_index in (1, 2, 3, 4):
        portion = lax.slice_in_dim(
            padded, tap_index * spacing, tap_index * spacing + length_out, axis=axis_number
        )
        summed = summed + SPLINE_TAPS[tap_index] * portion
    return summed


def depth_matrix(planes, spacing):
    matrix = np.zeros((planes, planes), np.float32)
    for tap_index in range(5):
        for i in range(planes):
            matrix[(i + (tap_index - 2) * spacing) % planes, i] += SPLINE_TAPS[tap_index]
    return matrix


def depth_pass(values_in, matrix):
    rows = values_in.shape[:-1]
    planes = values_in.shape[-1]
    flat = values_in.reshape(-1, planes)
    summed = jnp.dot(
        flat,
        jnp.asarray(matrix),
        precision=lax.Precision.HIGHEST,
        preferred_element_type=jnp.float32,
    )
    return summed.reshape(*rows, matrix.shape[1])


def moment_sums(detail):
    square = detail * detail
    return jnp.stack(
        [
            jnp.sum(jnp.abs(detail), axis=(0, 1)),
            jnp.sum(square, axis=(0, 1)),
            jnp.sum(square * detail, axis=(0, 1)),
            jnp.sum(square * square, axis=(0, 1)),
        ]
    )


def finish_table(table, planes):
    means = table / jnp.float32(SUB * SUB * planes)
    second = means[:, 1]
    third = means[:, 2] / (second + EPSILON) ** 1.5
    fourth = means[:, 3] / (second + EPSILON) ** 2
    return jnp.stack([means[:, 0], second, third, fourth], axis=1)


def gather_partials(partial, axes):
    count = 1
    for axis in axes:
        count *= lax.axis_size(axis)
    flat = partial.reshape(1, -1)
    sent = jnp.broadcast_to(flat, (count, flat.shape[1]))
    return lax.all_to_all(sent, axes, 0, 0, tiled=True)


def per_device(density):
    size_x, size_y, planes = density.shape
    assert SUB % size_x == 0 and SUB % size_y == 0
    assert len(SPACINGS) == 3
    first, second, third = SPACINGS
    matrix_1 = depth_matrix(planes, first)
    matrix_2 = depth_matrix(planes, second)
    matrix_3 = depth_matrix(planes, third)
    extra = 2 * second
    padded_y = padded_1(density, "col", 1, 2 * first)
    along_y = holed_pass(padded_y, first, 1, size_y)
    padded_x = padded_1(along_y, "row", 0, 2 * first + extra)
    along_x = holed_pass(padded_x, first, 0, size_x + 2 * extra)
    smooth_1 = depth_pass(lax.slice_in_dim(along_x, extra, extra + size_x, axis=0), matrix_1)
    along_x = depth_pass(holed_pass(along_x, second, 0, size_x), matrix_1 @ matrix_2)
    padded_y = padded_1(along_x, "col", 1, 2 * second)
    smooth_2 = holed_pass(padded_y, second, 1, size_y)
    ahead_3 = depth_pass(smooth_2, matrix_3)
    padded_y = padded_1(ahead_3, "col", 1, 2 * third)
    along_y = holed_pass(padded_y, third, 1, size_y)
    padded_x = padded_1(along_y, "row", 0, 2 * third)
    smooth_3 = holed_pass(padded_x, third, 0, size_x)
    current = smooth_3
    held = lax.optimization_barrier(((density, smooth_1), (smooth_1, smooth_2)))
    sums = [moment_sums(a - b) for a, b in held]
    sums.append(moment_sums(smooth_2 - smooth_3))
    partial = jnp.sum(jnp.stack(sums), axis=-1)
    count_x = lax.axis_size("row") * size_x // SUB
    count_y = lax.axis_size("col") * size_y // SUB
    gathered = gather_partials(partial, ("row", "col"))
    per_x = SUB // size_x
    per_y = SUB // size_y
    grouped = gathered.reshape(count_x, per_x, count_y, per_y, len(SPACINGS), 4)
    table = jnp.transpose(jnp.sum(grouped, axis=(1, 3)), (2, 3, 0, 1))
    return (current, finish_table(table, planes))


def solution(mesh):
    placed = (P("row", "col", None),)
    step = jax.shard_map(
        per_device,
        mesh=mesh,
        in_specs=placed,
        out_specs=(P("row", "col", None), P()),
        check_vma=False,
    )
    return step
```

```python
import jax
import jax.numpy as jnp
import numpy as np
from jax import lax
from jax.sharding import PartitionSpec as P

SUB = 256


SPLINE_TAPS = (0.0625, 0.25, 0.375, 0.25, 0.0625)
SPACINGS = (4, 8, 16)
EPSILON = 1e-06


def ring_pairs(count):
    forward = [(i, (i + 1) % count) for i in range(count)]
    backward = [(target, source) for source, target in forward]
    return forward, backward


def padded_1(block, axis, dim, width):
    count = lax.axis_size(axis)
    assert width <= block.shape[dim]
    forward, backward = ring_pairs(count)
    low = lax.ppermute(
        lax.slice_in_dim(block, block.shape[dim] - width, None, axis=dim), axis, forward
    )
    high = lax.ppermute(lax.slice_in_dim(block, 0, width, axis=dim), axis, backward)
    return jnp.concatenate([low, block, high], axis=dim)


def holed_pass(padded, spacing, axis_number, length_out):
    summed = SPLINE_TAPS[0] * lax.slice_in_dim(padded, 0, length_out, axis=axis_number)
    for tap_index in (1, 2, 3, 4):
        portion = lax.slice_in_dim(
            padded, tap_index * spacing, tap_index * spacing + length_out, axis=axis_number
        )
        summed = summed + SPLINE_TAPS[tap_index] * portion
    return summed


def depth_matrix(planes, spacing):
    matrix = np.zeros((planes, planes), np.float32)
    for tap_index in range(5):
        for i in range(planes):
            matrix[(i + (tap_index - 2) * spacing) % planes, i] += SPLINE_TAPS[tap_index]
    return matrix


def depth_pass(values_in, matrix):
    rows = values_in.shape[:-1]
    planes = values_in.shape[-1]
    flat = values_in.reshape(-1, planes)
    summed = jnp.dot(
        flat,
        jnp.asarray(matrix) if isinstance(matrix, np.ndarray) else matrix,
        precision=lax.Precision.HIGHEST,
        preferred_element_type=jnp.float32,
    )
    return summed.reshape(*rows, matrix.shape[1])


def moment_sums(detail):
    square = detail * detail
    return jnp.stack(
        [
            jnp.sum(jnp.abs(detail), axis=(0, 1)),
            jnp.sum(square, axis=(0, 1)),
            jnp.sum(square * detail, axis=(0, 1)),
            jnp.sum(square * square, axis=(0, 1)),
        ]
    )


def finish_table(table, planes):
    means = table / jnp.float32(SUB * SUB * planes)
    second = means[:, 1]
    third = means[:, 2] / (second + EPSILON) ** 1.5
    fourth = means[:, 3] / (second + EPSILON) ** 2
    return jnp.stack([means[:, 0], second, third, fourth], axis=1)


def gather_partials(partial, axes):
    count = 1
    for axis in axes:
        count *= lax.axis_size(axis)
    flat = partial.reshape(1, -1)
    sent = jnp.broadcast_to(flat, (count, flat.shape[1]))
    return lax.all_to_all(sent, axes, 0, 0, tiled=True)


def per_device(density):
    size_x, size_y, planes = density.shape
    assert SUB % size_x == 0 and SUB % size_y == 0
    assert len(SPACINGS) == 3
    first, second, third = SPACINGS
    matrix_1 = depth_matrix(planes, first)
    matrix_2 = depth_matrix(planes, second)
    matrix_3 = depth_matrix(planes, third)
    extra = 2 * second
    density, composed = lax.optimization_barrier((density, jnp.asarray(matrix_1 @ matrix_2)))
    padded_y = padded_1(density, "col", 1, 2 * first)
    along_y = holed_pass(padded_y, first, 1, size_y)
    padded_x = padded_1(along_y, "row", 0, 2 * first + extra)
    along_x = holed_pass(padded_x, first, 0, size_x + 2 * extra)
    smooth_1 = depth_pass(lax.slice_in_dim(along_x, extra, extra + size_x, axis=0), matrix_1)
    along_x = depth_pass(holed_pass(along_x, second, 0, size_x), composed)
    padded_y = padded_1(along_x, "col", 1, 2 * second)
    smooth_2 = holed_pass(padded_y, second, 1, size_y)
    ahead_3 = depth_pass(smooth_2, matrix_3)
    padded_y = padded_1(ahead_3, "col", 1, 2 * third)
    along_y = holed_pass(padded_y, third, 1, size_y)
    padded_x = padded_1(along_y, "row", 0, 2 * third)
    smooth_3 = holed_pass(padded_x, third, 0, size_x)
    current = smooth_3
    held = lax.optimization_barrier(((density, smooth_1), (smooth_1, smooth_2)))
    sums = [moment_sums(a - b) for a, b in held]
    sums.append(moment_sums(smooth_2 - smooth_3))
    partial = jnp.sum(jnp.stack(sums), axis=-1)
    count_x = lax.axis_size("row") * size_x // SUB
    count_y = lax.axis_size("col") * size_y // SUB
    gathered = gather_partials(partial, ("row", "col"))
    per_x = SUB // size_x
    per_y = SUB // size_y
    grouped = gathered.reshape(count_x, per_x, count_y, per_y, len(SPACINGS), 4)
    table = jnp.transpose(jnp.sum(grouped, axis=(1, 3)), (2, 3, 0, 1))
    return (current, finish_table(table, planes))


def solution(mesh):
    placed = (P("row", "col", None),)
    step = jax.shard_map(
        per_device,
        mesh=mesh,
        in_specs=placed,
        out_specs=(P("row", "col", None), P()),
        check_vma=False,
    )
    return step
```
